32 devices in a mesh: grp: 2 (over y), tm: 4 (over z), freq: 4 (over x, core).
Axes of the slice: x: 2, y: 2, z: 4, core: 2. Of those that a mesh axis runs over, the one named last changes fastest.
Arguments:
- visibilities: bfloat16 [2, 132, 64, 1536], P(None, 'grp', 'tm', 'freq'), parts along dimension 1, may hold values from -6 to 6
- class_ids: int32 [132], P('grp'), parts along dimension 0, may hold values from 0 to 3, as said below
- class_counts: int32 [8], P('grp'), parts along dimension 0, may hold values from 1 to 32, as said below
- tap_windows: int32 [8], P('grp'), parts along dimension 0, may hold values from 1 to 4, as said below
- fringe_taps: float32 [2, 8, 9], P(None, 'grp'), parts along dimension 1, may hold values from -2.4 to 2.4
- flag_mask: int32 [64, 1536], P('freq'), may hold values 0 or 1
- filter_panels: bfloat16 [8, 1536, 1536], P(('grp', 'tm'), 'freq'), parts along dimension 0
Outputs:
- cleaned: bfloat16 [2, 8, 32, 64, 1536], P(None, ('grp', 'tm'), None, 'freq'), parts along dimension 1
The draws below stay inside these ranges and needn't reach their ends.
There are 2 independent parts, one for each index of `grp`. The reference program is written for one: setup_inputs(seed, part) draws one part's arguments, and reference() takes and returns one part's arrays. A program takes and returns all parts, laid end to end along the dimension named above; an argument that names none is the same for every part. Nothing has to cross between parts.
Inputs may be any that keep to these rules, and one draw needn't show every extreme that they name: Baselines are listed grouped by class in increasing order of class; class_ids[b] is the class of baseline b. class_counts[c] is the number of baselines whose class is c; some class has exactly 32 baselines. `tap_windows`: some class has a window of exactly 4.
All inputs are finite; a program needn't handle non-finite values. No bound on the sum of `flag_mask` on one device may be relied on, other than what follows from the above.
Results may differ from the reference program's by a relative error of at most 0.0049.
Values may be sent and summed in bfloat16 or wider, within the bound.
No kernel may reach another device: no remote copies, remote signals or barrier semaphores. Data moves between devices by JAX's collectives and lax.ppermute only.
A program may use at most 128 MiB of HBM per device.

```python
import jax
import jax.numpy as jnp
from jax import lax

CHANNEL_COUNT = 1536
SLOTS = 32
REACH = 4
CLASSES = 4
BASELINE_COUNT = 66
TIME_STEPS = 64


def class_layout(key):
    first_member = jax.random.randint(jax.random.fold_in(key, 11), (CLASSES // 2,), 1, SLOTS + 1)
    first_member = first_member.at[0].set(SLOTS)
    paired = jnp.stack([first_member, SLOTS + 1 - first_member], axis=1).reshape(-1)
    class_order = jax.random.permutation(jax.random.fold_in(key, 12), CLASSES)
    return paired[class_order].astype(jnp.int32)


def draw_class_counts(key, part):
    return class_layout(key)


def draw_class_ids(key, part):
    class_ends = jnp.cumsum(class_layout(key))
    baseline_positions = jnp.arange(BASELINE_COUNT, dtype=jnp.int32)
    return jnp.sum((baseline_positions[:, None] >= class_ends[None, :]).astype(jnp.int32), axis=1).astype(jnp.int32)


def draw_tap_windows(key, part):
    window_base = jax.random.randint(jax.random.fold_in(key, 21), (CLASSES,), 1, REACH + 1)
    widest = jax.random.randint(jax.random.fold_in(key, 22), (), 0, CLASSES)
    return jnp.where(jnp.arange(CLASSES, dtype=jnp.int32) == widest, REACH, window_base).astype(jnp.int32)


def draw_filter_panels(key, part):
    spread = jax.random.normal(jax.random.fold_in(key, 31), (CLASSES, CHANNEL_COUNT, CHANNEL_COUNT), jnp.float32)
    diagonal_level = jax.random.uniform(jax.random.fold_in(key, 32), (CLASSES, CHANNEL_COUNT), jnp.float32, 0.3, 0.7)
    channel_iota = jnp.arange(CHANNEL_COUNT, dtype=jnp.int32)
    identity_part = (channel_iota[:, None] == channel_iota[None, :]).astype(jnp.float32)
    panels_full = spread * (0.5 / CHANNEL_COUNT ** 0.5) + identity_part[None, :, :] * diagonal_level[:, :, None]
    return panels_full.astype(jnp.bfloat16)


def place_ends(array, own_key, smallest, largest):
    place = [jax.random.randint(jax.random.fold_in(own_key, axis), (), 0, length) for axis, length in enumerate(array.shape)]
    main_axis = array.shape.index(max(array.shape))
    next_to = place[:main_axis] + [(place[main_axis] + 1) % array.shape[main_axis]] + place[main_axis + 1:]
    return array.at[tuple(place)].set(smallest).at[tuple(next_to)].set(largest)


def steps_of(rng, dims, split, smallest, largest):
    gain, own = 1.0, jax.random.fold_in(rng, 6)
    for position, parts in split:
        draws = jnp.exp(jax.random.uniform(jax.random.fold_in(own, position), (parts,), jnp.float32, smallest / len(split), largest / len(split)))
        gain = gain * jnp.repeat(draws, dims[position] // parts).reshape([-1 if axis == position else 1 for axis in range(len(dims))])
    return gain


def noise(stream_key, shape, scale, most, shards=(), kind=jnp.bfloat16):
    entries = jax.random.normal(stream_key, shape, jnp.float32) * scale
    if len(shards) > 0:
        entries = steps_of(stream_key, shape, shards, -0.22, 0.18) * entries
    return jnp.clip(entries, min=-most, max=most).astype(kind)


def setup_inputs(seed: int = 0, part: int = 0) -> dict:
    keys = jax.random.split(jax.random.key(seed), 8)
    part_splits = jax.random.split(jax.random.fold_in(keys[7], part), 8)
    visibilities = noise(part_splits[0], (2, BASELINE_COUNT, TIME_STEPS, CHANNEL_COUNT), 1.0, 6.0, ((2, 4), (3, 4)))
    class_ids = draw_class_ids(jax.random.fold_in(jax.random.fold_in(keys[7], part), 71), part)
    class_counts = draw_class_counts(jax.random.fold_in(jax.random.fold_in(keys[7], part), 71), part)
    tap_windows = draw_tap_windows(jax.random.fold_in(jax.random.fold_in(keys[7], part), 71), part)
    fringe_taps = noise(part_splits[4], (2, CLASSES, 2 * REACH + 1), 0.4, 2.4, (), jnp.float32)
    flag_mask = place_ends((jax.random.randint(keys[5], (TIME_STEPS, CHANNEL_COUNT), 0, 8) < 7).astype(jnp.int32), jax.random.fold_in(keys[5], 1), 0, 1)
    filter_panels = draw_filter_panels(jax.random.fold_in(jax.random.fold_in(keys[7], part), 71), part)
    return dict(visibilities=visibilities, class_ids=class_ids, class_counts=class_counts, tap_windows=tap_windows, fringe_taps=fringe_taps, flag_mask=flag_mask, filter_panels=filter_panels)


def masked_taps(fringe_taps, tap_windows):
    offsets = jnp.abs(jnp.arange(2 * REACH + 1, dtype=jnp.int32) - REACH)
    keep = (offsets[None, :] <= tap_windows[:, None]).astype(jnp.float32)
    return fringe_taps * keep[None, :, :]


def reference(visibilities, class_ids, class_counts, tap_windows, fringe_taps, flag_mask, filter_panels):
    row_taps = masked_taps(fringe_taps, tap_windows)[:, class_ids, :]
    padded = jnp.pad(visibilities.astype(jnp.float32), ((0, 0), (0, 0), (REACH, REACH), (0, 0)))
    real_part = jnp.zeros(visibilities.shape[1:], jnp.float32)
    imag_part = jnp.zeros(visibilities.shape[1:], jnp.float32)
    for offset in range(2 * REACH + 1):
        shifted = padded[:, :, 2 * REACH - offset:2 * REACH - offset + TIME_STEPS, :]
        tap_real = row_taps[0, :, offset][:, None, None]
        tap_imag = row_taps[1, :, offset][:, None, None]
        real_part = real_part + tap_real * shifted[0] - tap_imag * shifted[1]
        imag_part = imag_part + tap_real * shifted[1] + tap_imag * shifted[0]
    filtered = jnp.stack([real_part, imag_part]).astype(jnp.bfloat16)
    class_starts = jnp.cumsum(class_counts) - class_counts
    flag_gate = flag_mask.astype(jnp.bfloat16)
    slot_positions = jnp.arange(SLOTS, dtype=jnp.int32)

    def one_class(class_number_index):
        input_visibility = jnp.clip(class_starts[class_number_index] + slot_positions, 0, BASELINE_COUNT - 1).astype(jnp.int32)
        live_slot = slot_positions < class_counts[class_number_index]
        slot_rows = jnp.take(filtered, input_visibility, axis=1)
        slot_rows = jnp.where(live_slot[None, :, None, None], slot_rows, jnp.zeros((), jnp.bfloat16))
        weighted = slot_rows * flag_gate
        dayenu_fit = jnp.einsum("rstj,ij->rsti", weighted.astype(jnp.float32), filter_panels[class_number_index].astype(jnp.float32))
        return (slot_rows.astype(jnp.float32) - dayenu_fit).astype(jnp.bfloat16)

    cleaned = lax.map(one_class, jnp.arange(CLASSES, dtype=jnp.int32))
    return jnp.moveaxis(cleaned, 0, 1)
```

```python
import jax
import jax.numpy as jnp
from jax import lax
from jax.sharding import PartitionSpec as P

SLOTS = 32
REACH = 4


def extended(cells, sides, width):
    for axis, dim in sides:
        count = lax.axis_size(axis)
        ends = count - 1
        head = lax.slice_in_dim(cells, 0, width, axis=dim)
        tail = lax.slice_in_dim(cells, cells.shape[dim] - width, cells.shape[dim], axis=dim)
        cells = jnp.concatenate(
            [
                lax.ppermute(tail, axis, [(i, (i + 1) % count) for i in range(ends)]),
                cells,
                lax.ppermute(head, axis, [((i + 1) % count, i) for i in range(ends)]),
            ],
            axis=dim,
        )
    return cells


def masked_taps(fringe_taps, tap_windows):
    offsets = jnp.abs(jnp.arange(2 * REACH + 1, dtype=jnp.int32) - REACH)
    keep = (offsets[None, :] <= tap_windows[:, None]).astype(jnp.float32)
    return fringe_taps * keep[None, :, :]


def convolve(rows, slot_taps, length):
    real_part = jnp.zeros(rows.shape[1:2] + (length,) + rows.shape[3:], jnp.float32)
    imag_part = jnp.zeros_like(real_part)
    for offset in range(2 * REACH + 1):
        shifted = lax.slice_in_dim(rows, 2 * REACH - offset, 2 * REACH - offset + length, axis=2)
        shifted = shifted.astype(jnp.float32)
        tap_real = slot_taps[0, :, offset][:, None, None]
        tap_imag = slot_taps[1, :, offset][:, None, None]
        real_part = real_part + tap_real * shifted[0] - tap_imag * shifted[1]
        imag_part = imag_part + tap_real * shifted[1] + tap_imag * shifted[0]
    return jnp.stack([real_part, imag_part]).astype(jnp.bfloat16)


def to_slots(per_baseline, class_counts):
    class_starts = jnp.cumsum(class_counts) - class_counts
    slot_positions = jnp.arange(SLOTS, dtype=jnp.int32)
    input_visibility = jnp.clip(
        class_starts[:, None] + slot_positions[None, :], 0, per_baseline.shape[1] - 1
    )
    live_slot = slot_positions[None, :] < class_counts[:, None]
    gathered = jnp.take(per_baseline, input_visibility.reshape(-1), axis=1)
    gathered = gathered.reshape(per_baseline.shape[:1] + live_slot.shape + per_baseline.shape[2:])
    return jnp.where(live_slot[None, :, :, None, None], gathered, jnp.zeros((), per_baseline.dtype))


def two_stage(
    visibilities, class_ids, class_counts, tap_windows, fringe_taps, flag_mask, filter_panels
):
    taps_kept = masked_taps(fringe_taps, tap_windows)
    padded = extended(visibilities, (("tm", 2),), REACH)
    row_taps = taps_kept[:, class_ids, :]
    filtered = convolve(padded, row_taps, visibilities.shape[2])
    slotted = to_slots(filtered, class_counts)
    local_block = lax.all_to_all(
        lax.all_to_all(slotted, "tm", split_axis=1, concat_axis=3, tiled=True),
        "freq",
        split_axis=3,
        concat_axis=4,
        tiled=True,
    )
    weighted = local_block * flag_mask.astype(jnp.bfloat16)
    dayenu_fit = jnp.einsum(
        "rcstj,cij->rcsti",
        weighted,
        lax.all_gather(filter_panels, "freq", axis=1, tiled=True),
        preferred_element_type=jnp.float32,
    )
    return (local_block.astype(jnp.float32) - dayenu_fit).astype(jnp.bfloat16)


def shards(
    visibilities, class_ids, class_counts, tap_windows, fringe_taps, flag_mask, filter_panels
):
    nt = lax.axis_size("tm")
    nf = lax.axis_size("freq")
    if nt != nf:
        return two_stage(
            visibilities, class_ids, class_counts, tap_windows, fringe_taps, flag_mask,
            filter_panels,
        )
    q = nt // nf
    a = lax.axis_index("tm")
    b = lax.axis_index("freq")
    baselines = visibilities.shape[1]
    t_in = visibilities.shape[2]
    f_blk = visibilities.shape[3]
    t_out = flag_mask.shape[0]
    channels = flag_mask.shape[1]

    taps_kept = masked_taps(fringe_taps, tap_windows)
    class_starts = jnp.cumsum(class_counts) - class_counts
    slot_positions = jnp.arange(SLOTS, dtype=jnp.int32)

    padded = extended(visibilities, (("tm", 2),), REACH)
    padded = jnp.pad(padded, ((0, 0), (0, SLOTS), (0, 0), (0, 0)))

    panel = lax.all_gather(filter_panels[0], "freq", axis=0, tiled=True)
    panel = panel.reshape(channels, nf, f_blk)

    c_own = a
    u_src = (a % q) * nf + b
    fit = jnp.zeros((2, SLOTS, t_out, channels), jnp.float32)
    slotted = jnp.zeros((2, SLOTS, t_out, channels), jnp.bfloat16)
    for r in range(nt):
        c_send = (u_src + r) % nt
        start = class_starts[c_send]
        rows = lax.dynamic_slice_in_dim(padded, start, SLOTS, axis=1)
        row_ids = jnp.clip(start + slot_positions, 0, baselines - 1)
        slot_taps = taps_kept[:, class_ids[row_ids], :]
        chunk = convolve(rows, slot_taps, t_in)
        live = slot_positions < class_counts[c_send]
        chunk = jnp.where(live[None, :, None, None], chunk, jnp.zeros((), chunk.dtype))
        perm = []
        for sa in range(nt):
            for sb in range(nf):
                u = (sa % q) * nf + sb
                dc = (u + r) % nt
                perm.append((sa * nf + sb, dc * nf + sa // q))
        got = lax.ppermute(chunk, ("tm", "freq"), perm)
        u_dst = (c_own - r) % nt
        t_sub = u_dst // nf
        b_src = u_dst % nf
        gate = lax.dynamic_slice(flag_mask, (t_sub * t_in, b_src * f_blk), (t_in, f_blk))
        weighted = got * gate.astype(jnp.bfloat16)
        cols = lax.dynamic_index_in_dim(panel, b_src, axis=1, keepdims=False)
        part = jnp.einsum("rstj,ij->rsti", weighted, cols, preferred_element_type=jnp.float32)
        if q == 1:
            fit = fit + part
        else:
            prev = lax.dynamic_slice_in_dim(fit, t_sub * t_in, t_in, axis=2)
            fit = lax.dynamic_update_slice_in_dim(fit, prev + part, t_sub * t_in, axis=2)
        slotted = lax.dynamic_update_slice(slotted, got, (0, 0, t_sub * t_in, b_src * f_blk))
    cleaned = (slotted.astype(jnp.float32) - fit).astype(jnp.bfloat16)
    return cleaned[:, None]


def solution(mesh):
    return jax.shard_map(
        shards,
        mesh=mesh,
        in_specs=(
            P(None, "grp", "tm", "freq"),
            P("grp"),
            P("grp"),
            P("grp"),
            P(None, "grp", None),
            P("freq", None),
            P(("grp", "tm"), "freq", None),
        ),
        out_specs=P(None, ("grp", "tm"), None, "freq", None),
        check_vma=False,
    )
```

```python
import jax
import jax.numpy as jnp
from jax import lax
from jax.sharding import PartitionSpec as P

SLOTS = 32
REACH = 4


def extended(cells, sides, width):
    for axis, dim in sides:
        count = lax.axis_size(axis)
        ends = count - 1
        head = lax.slice_in_dim(cells, 0, width, axis=dim)
        tail = lax.slice_in_dim(cells, cells.shape[dim] - width, cells.shape[dim], axis=dim)
        cells = jnp.concatenate(
            [
                lax.ppermute(tail, axis, [(i, (i + 1) % count) for i in range(ends)]),
                cells,
                lax.ppermute(head, axis, [((i + 1) % count, i) for i in range(ends)]),
            ],
            axis=dim,
        )
    return cells


def masked_taps(fringe_taps, tap_windows):
    offsets = jnp.abs(jnp.arange(2 * REACH + 1, dtype=jnp.int32) - REACH)
    keep = (offsets[None, :] <= tap_windows[:, None]).astype(jnp.float32)
    return fringe_taps * keep[None, :, :]


def convolve(rows, slot_taps, length):
    real_part = jnp.zeros(rows.shape[1:2] + (length,) + rows.shape[3:], jnp.float32)
    imag_part = jnp.zeros_like(real_part)
    for offset in range(2 * REACH + 1):
        shifted = lax.slice_in_dim(rows, 2 * REACH - offset, 2 * REACH - offset + length, axis=2)
        tap_real = slot_taps[0, :, offset][:, None, None]
        tap_imag = slot_taps[1, :, offset][:, None, None]
        real_part = real_part + tap_real * shifted[0] - tap_imag * shifted[1]
        imag_part = imag_part + tap_real * shifted[1] + tap_imag * shifted[0]
    return jnp.stack([real_part, imag_part]).astype(jnp.bfloat16)


def to_slots(per_baseline, class_counts):
    class_starts = jnp.cumsum(class_counts) - class_counts
    slot_positions = jnp.arange(SLOTS, dtype=jnp.int32)
    input_visibility = jnp.clip(
        class_starts[:, None] + slot_positions[None, :], 0, per_baseline.shape[1] - 1
    )
    live_slot = slot_positions[None, :] < class_counts[:, None]
    gathered = jnp.take(per_baseline, input_visibility.reshape(-1), axis=1)
    gathered = gathered.reshape(per_baseline.shape[:1] + live_slot.shape + per_baseline.shape[2:])
    return jnp.where(live_slot[None, :, :, None, None], gathered, jnp.zeros((), per_baseline.dtype))


def two_stage(
    visibilities, class_ids, class_counts, tap_windows, fringe_taps, flag_mask, filter_panels
):
    taps_kept = masked_taps(fringe_taps, tap_windows)
    padded = extended(visibilities, (("tm", 2),), REACH)
    row_taps = taps_kept[:, class_ids, :]
    filtered = convolve(padded, row_taps, visibilities.shape[2])
    slotted = to_slots(filtered, class_counts)
    local_block = lax.all_to_all(
        lax.all_to_all(slotted, "tm", split_axis=1, concat_axis=3, tiled=True),
        "freq",
        split_axis=3,
        concat_axis=4,
        tiled=True,
    )
    weighted = local_block * flag_mask.astype(jnp.bfloat16)
    dayenu_fit = jnp.einsum(
        "rcstj,cij->rcsti",
        weighted,
        lax.all_gather(filter_panels, "freq", axis=1, tiled=True),
        preferred_element_type=jnp.float32,
    )
    return (local_block.astype(jnp.float32) - dayenu_fit).astype(jnp.bfloat16)


def shards(
    visibilities, class_ids, class_counts, tap_windows, fringe_taps, flag_mask, filter_panels
):
    nt = lax.axis_size("tm")
    nf = lax.axis_size("freq")
    if nt != nf:
        return two_stage(
            visibilities, class_ids, class_counts, tap_windows, fringe_taps, flag_mask,
            filter_panels,
        )
    q = nt // nf
    a = lax.axis_index("tm")
    b = lax.axis_index("freq")
    baselines = visibilities.shape[1]
    t_in = visibilities.shape[2]
    f_blk = visibilities.shape[3]
    t_out = flag_mask.shape[0]
    channels = flag_mask.shape[1]

    taps_kept = masked_taps(fringe_taps, tap_windows)
    class_starts = jnp.cumsum(class_counts) - class_counts
    slot_positions = jnp.arange(SLOTS, dtype=jnp.int32)

    padded = extended(visibilities, (("tm", 2),), REACH)
    padded = jnp.pad(padded, ((0, 0), (0, SLOTS), (0, 0), (0, 0)))

    panel = lax.all_gather(filter_panels[0], "freq", axis=0, tiled=True)
    if q == 1:
        shift = ((a + 1) % nf) * f_blk
        panel = lax.dynamic_slice_in_dim(jnp.concatenate([panel, panel], axis=1), shift, channels, axis=1)

    c_own = a
    u_src = (a % q) * nf + b
    fit = None
    received = []
    for r in range(nt):
        c_send = (u_src + r) % nt
        start = class_starts[c_send]
        rows = lax.optimization_barrier(lax.dynamic_slice_in_dim(padded, start, SLOTS, axis=1))
        row_ids = jnp.clip(start + slot_positions, 0, baselines - 1)
        slot_taps = taps_kept[:, class_ids[row_ids], :]
        chunk = convolve(rows, slot_taps, t_in)
        live = slot_positions < class_counts[c_send]
        chunk = jnp.where(live[None, :, None, None], chunk, jnp.zeros((), chunk.dtype))
        perm = []
        for sa in range(nt):
            for sb in range(nf):
                u = (sa % q) * nf + sb
                dc = (u + r) % nt
                perm.append((sa * nf + sb, dc * nf + sa // q))
        got = lax.ppermute(chunk, ("tm", "freq"), perm)
        u_dst = (c_own - r) % nt
        t_sub = u_dst // nf
        b_src = u_dst % nf
        if q == 1:
            gate = lax.dynamic_slice_in_dim(flag_mask, b_src * f_blk, f_blk, axis=1)
            cols = lax.slice_in_dim(panel, (nf - 1 - r) * f_blk, (nf - r) * f_blk, axis=1)
        else:
            gate = lax.dynamic_slice(flag_mask, (t_sub * t_in, b_src * f_blk), (t_in, f_blk))
            cols = lax.dynamic_slice_in_dim(panel, b_src * f_blk, f_blk, axis=1)
        weighted = got * gate.astype(jnp.bfloat16)
        part = jnp.einsum("rstj,ij->rsti", weighted, cols, preferred_element_type=jnp.float32)
        if q == 1:
            fit = part if fit is None else fit + part
            received.append(got)
        else:
            if fit is None:
                fit = jnp.zeros((2, SLOTS, t_out, channels), jnp.float32)
                slotted = jnp.zeros((2, SLOTS, t_out, channels), jnp.bfloat16)
            prev = lax.dynamic_slice_in_dim(fit, t_sub * t_in, t_in, axis=2)
            fit = lax.dynamic_update_slice_in_dim(fit, prev + part, t_sub * t_in, axis=2)
            slotted = lax.dynamic_update_slice(slotted, got, (0, 0, t_sub * t_in, b_src * f_blk))
    if q == 1:
        stacked = jnp.stack(received)
        slotted = jnp.concatenate(
            [lax.dynamic_index_in_dim(stacked, (a - k) % nf, 0, keepdims=False) for k in range(nf)],
            axis=3,
        )
    cleaned = (slotted.astype(jnp.float32) - fit).astype(jnp.bfloat16)
    return cleaned[:, None]


def solution(mesh):
    return jax.shard_map(
        shards,
        mesh=mesh,
        in_specs=(
            P(None, "grp", "tm", "freq"),
            P("grp"),
            P("grp"),
            P("grp"),
            P(None, "grp", None),
            P("freq", None),
            P(("grp", "tm"), "freq", None),
        ),
        out_specs=P(None, ("grp", "tm"), None, "freq", None),
        check_vma=False,
    )
```

```python
import jax
import jax.numpy as jnp
from jax import lax
from jax.sharding import PartitionSpec as P


SLOTS = 32
REACH = 4


def extended(cells, sides, width):
    for axis, dim in sides:
        count = lax.axis_size(axis)
        ends = count - 1
        head = lax.slice_in_dim(cells, 0, width, axis=dim)
        tail = lax.slice_in_dim(cells, cells.shape[dim] - width, cells.shape[dim], axis=dim)
        cells = jnp.concatenate(
            [
                lax.ppermute(tail, axis, [(i, (i + 1) % count) for i in range(ends)]),
                cells,
                lax.ppermute(head, axis, [((i + 1) % count, i) for i in range(ends)]),
            ],
            axis=dim,
        )
    return cells


def masked_taps(fringe_taps, tap_windows):
    offsets = jnp.abs(jnp.arange(2 * REACH + 1, dtype=jnp.int32) - REACH)
    keep = (offsets[None, :] <= tap_windows[:, None]).astype(jnp.float32)
    return fringe_taps * keep[None, :, :]


def convolve(rows, slot_taps, length):
    real_part = jnp.zeros(rows.shape[1:2] + (length,) + rows.shape[3:], jnp.float32)
    imag_part = jnp.zeros_like(real_part)
    for offset in range(2 * REACH + 1):
        shifted = lax.slice_in_dim(rows, 2 * REACH - offset, 2 * REACH - offset + length, axis=2)
        tap_real = slot_taps[0, :, offset][:, None, None]
        tap_imag = slot_taps[1, :, offset][:, None, None]
        real_part = real_part + tap_real * shifted[0] - tap_imag * shifted[1]
        imag_part = imag_part + tap_real * shifted[1] + tap_imag * shifted[0]
    return jnp.stack([real_part, imag_part]).astype(jnp.bfloat16)


def convolve_class(rows, taps, count, length):
    real_part = jnp.zeros(rows.shape[1:2] + (length,) + rows.shape[3:], jnp.float32)
    imag_part = jnp.zeros_like(real_part)
    for offset in range(2 * REACH + 1):
        shifted = lax.slice_in_dim(rows, 2 * REACH - offset, 2 * REACH - offset + length, axis=2)
        real_part = real_part + taps[0, offset] * shifted[0] - taps[1, offset] * shifted[1]
        imag_part = imag_part + taps[0, offset] * shifted[1] + taps[1, offset] * shifted[0]
    out = jnp.stack([real_part, imag_part])
    live = lax.broadcasted_iota(jnp.int32, out.shape, 1) < count
    return jnp.where(live, out, 0.0).astype(jnp.bfloat16)


def to_slots(per_baseline, class_counts):
    class_starts = jnp.cumsum(class_counts) - class_counts
    slot_positions = jnp.arange(SLOTS, dtype=jnp.int32)
    input_visibility = jnp.clip(
        class_starts[:, None] + slot_positions[None, :], 0, per_baseline.shape[1] - 1
    )
    live_slot = slot_positions[None, :] < class_counts[:, None]
    gathered = jnp.take(per_baseline, input_visibility.reshape(-1), axis=1)
    gathered = gathered.reshape(per_baseline.shape[:1] + live_slot.shape + per_baseline.shape[2:])
    return jnp.where(live_slot[None, :, :, None, None], gathered, jnp.zeros((), per_baseline.dtype))


def two_stage(
    visibilities, class_ids, class_counts, tap_windows, fringe_taps, flag_mask, filter_panels
):
    taps_kept = masked_taps(fringe_taps, tap_windows)
    padded = extended(visibilities, (("tm", 2),), REACH)
    row_taps = taps_kept[:, class_ids, :]
    filtered = convolve(padded, row_taps, visibilities.shape[2])
    slotted = to_slots(filtered, class_counts)
    local_block = lax.all_to_all(
        lax.all_to_all(slotted, "tm", split_axis=1, concat_axis=3, tiled=True),
        "freq",
        split_axis=3,
        concat_axis=4,
        tiled=True,
    )
    weighted = local_block * flag_mask.astype(jnp.bfloat16)
    dayenu_fit = jnp.einsum(
        "rcstj,cij->rcsti",
        weighted,
        lax.all_gather(filter_panels, "freq", axis=1, tiled=True),
        preferred_element_type=jnp.float32,
    )
    return (local_block.astype(jnp.float32) - dayenu_fit).astype(jnp.bfloat16)


def shards(
    visibilities, class_ids, class_counts, tap_windows, fringe_taps, flag_mask, filter_panels
):
    nt = lax.axis_size("tm")
    nf = lax.axis_size("freq")
    if nt != nf:
        return two_stage(
            visibilities, class_ids, class_counts, tap_windows, fringe_taps, flag_mask,
            filter_panels,
        )
    q = nt // nf
    a = lax.axis_index("tm")
    b = lax.axis_index("freq")
    t_in = visibilities.shape[2]
    f_blk = visibilities.shape[3]
    t_out = flag_mask.shape[0]
    channels = flag_mask.shape[1]

    taps_kept = masked_taps(fringe_taps, tap_windows)
    class_starts = jnp.cumsum(class_counts) - class_counts

    padded = extended(visibilities, (("tm", 2),), REACH)
    padded = jnp.pad(padded, ((0, 0), (0, SLOTS), (0, 0), (0, 0)))

    panel = lax.all_gather(filter_panels[0], "freq", axis=0, tiled=True)
    if q == 1:
        shift = ((a + 1) % nf) * f_blk
        panel = lax.dynamic_slice_in_dim(jnp.concatenate([panel, panel], axis=1), shift, channels, axis=1)

    c_own = a
    u_src = (a % q) * nf + b
    fit = None
    for r in range(nt):
        c_send = (u_src + r) % nt
        start = class_starts[c_send]
        rows = lax.optimization_barrier(lax.dynamic_slice_in_dim(padded, start, SLOTS, axis=1))
        taps = lax.dynamic_index_in_dim(taps_kept, c_send, axis=1, keepdims=False)
        chunk = convolve_class(rows, taps, class_counts[c_send], t_in)
        perm = []
        for sa in range(nt):
            for sb in range(nf):
                u = (sa % q) * nf + sb
                dc = (u + r) % nt
                perm.append((sa * nf + sb, dc * nf + sa // q))
        got = lax.ppermute(chunk, ("tm", "freq"), perm)
        u_dst = (c_own - r) % nt
        t_sub = u_dst // nf
        b_src = u_dst % nf
        if q == 1:
            gate = lax.dynamic_slice_in_dim(flag_mask, b_src * f_blk, f_blk, axis=1)
            cols = lax.slice_in_dim(panel, (nf - 1 - r) * f_blk, (nf - r) * f_blk, axis=1)
        else:
            gate = lax.dynamic_slice(flag_mask, (t_sub * t_in, b_src * f_blk), (t_in, f_blk))
            cols = lax.dynamic_slice_in_dim(panel, b_src * f_blk, f_blk, axis=1)
        weighted = got * gate.astype(jnp.bfloat16)
        part = jnp.einsum("rstj,ij->rsti", weighted, cols, preferred_element_type=jnp.float32)
        if fit is None:
            slotted = jnp.zeros((2, SLOTS, t_out, channels), jnp.bfloat16)
        if q == 1:
            fit = part if fit is None else fit + part
            slotted = lax.dynamic_update_slice_in_dim(slotted, got, b_src * f_blk, axis=3)
        else:
            if fit is None:
                fit = jnp.zeros((2, SLOTS, t_out, channels), jnp.float32)
            prev = lax.dynamic_slice_in_dim(fit, t_sub * t_in, t_in, axis=2)
            fit = lax.dynamic_update_slice_in_dim(fit, prev + part, t_sub * t_in, axis=2)
            slotted = lax.dynamic_update_slice(slotted, got, (0, 0, t_sub * t_in, b_src * f_blk))
    cleaned = (slotted.astype(jnp.float32) - fit).astype(jnp.bfloat16)
    return cleaned[:, None]


def solution(mesh):
    return jax.shard_map(
        shards,
        mesh=mesh,
        in_specs=(
            P(None, "grp", "tm", "freq"),
            P("grp"),
            P("grp"),
            P("grp"),
            P(None, "grp", None),
            P("freq", None),
            P(("grp", "tm"), "freq", None),
        ),
        out_specs=P(None, ("grp", "tm"), None, "freq", None),
        check_vma=False,
    )
```

```python
import jax
import jax.numpy as jnp
from jax import lax
from jax.sharding import PartitionSpec as P


SLOTS = 32
REACH = 4


def extended(cells, sides, width):
    for axis, dim in sides:
        count = lax.axis_size(axis)
        ends = count - 1
        head = lax.slice_in_dim(cells, 0, width, axis=dim)
        tail = lax.slice_in_dim(cells, cells.shape[dim] - width, cells.shape[dim], axis=dim)
        cells = jnp.concatenate(
            [
                lax.ppermute(tail, axis, [(i, (i + 1) % count) for i in range(ends)]),
                cells,
                lax.ppermute(head, axis, [((i + 1) % count, i) for i in range(ends)]),
            ],
            axis=dim,
        )
    return cells


def masked_taps(fringe_taps, tap_windows):
    offsets = jnp.abs(jnp.arange(2 * REACH + 1, dtype=jnp.int32) - REACH)
    keep = (offsets[None, :] <= tap_windows[:, None]).astype(jnp.float32)
    return fringe_taps * keep[None, :, :]


def convolve(rows, slot_taps, length):
    real_part = jnp.zeros(rows.shape[1:2] + (length,) + rows.shape[3:], jnp.float32)
    imag_part = jnp.zeros_like(real_part)
    for offset in range(2 * REACH + 1):
        shifted = lax.slice_in_dim(rows, 2 * REACH - offset, 2 * REACH - offset + length, axis=2)
        tap_real = slot_taps[0, :, offset][:, None, None]
        tap_imag = slot_taps[1, :, offset][:, None, None]
        real_part = real_part + tap_real * shifted[0] - tap_imag * shifted[1]
        imag_part = imag_part + tap_real * shifted[1] + tap_imag * shifted[0]
    return jnp.stack([real_part, imag_part]).astype(jnp.bfloat16)


def convolve_class(rows, taps, count, length):
    live = (jnp.arange(rows.shape[1], dtype=jnp.int32) < count).astype(jnp.float32)
    return convolve(rows, taps[:, None, :] * live[None, :, None], length)


def to_slots(per_baseline, class_counts):
    class_starts = jnp.cumsum(class_counts) - class_counts
    slot_positions = jnp.arange(SLOTS, dtype=jnp.int32)
    input_visibility = jnp.clip(
        class_starts[:, None] + slot_positions[None, :], 0, per_baseline.shape[1] - 1
    )
    live_slot = slot_positions[None, :] < class_counts[:, None]
    gathered = jnp.take(per_baseline, input_visibility.reshape(-1), axis=1)
    gathered = gathered.reshape(per_baseline.shape[:1] + live_slot.shape + per_baseline.shape[2:])
    return jnp.where(live_slot[None, :, :, None, None], gathered, jnp.zeros((), per_baseline.dtype))


def two_stage(
    visibilities, class_ids, class_counts, tap_windows, fringe_taps, flag_mask, filter_panels
):
    taps_kept = masked_taps(fringe_taps, tap_windows)
    padded = extended(visibilities, (("tm", 2),), REACH)
    row_taps = taps_kept[:, class_ids, :]
    filtered = convolve(padded, row_taps, visibilities.shape[2])
    slotted = to_slots(filtered, class_counts)
    local_block = lax.all_to_all(
        lax.all_to_all(slotted, "tm", split_axis=1, concat_axis=3, tiled=True),
        "freq",
        split_axis=3,
        concat_axis=4,
        tiled=True,
    )
    weighted = local_block * flag_mask.astype(jnp.bfloat16)
    dayenu_fit = jnp.einsum(
        "rcstj,cij->rcsti",
        weighted,
        lax.all_gather(filter_panels, "freq", axis=1, tiled=True),
        preferred_element_type=jnp.float32,
    )
    return (local_block.astype(jnp.float32) - dayenu_fit).astype(jnp.bfloat16)


def shards(
    visibilities, class_ids, class_counts, tap_windows, fringe_taps, flag_mask, filter_panels
):
    nt = lax.axis_size("tm")
    nf = lax.axis_size("freq")
    if nt != nf:
        return two_stage(
            visibilities, class_ids, class_counts, tap_windows, fringe_taps, flag_mask,
            filter_panels,
        )
    q = nt // nf
    a = lax.axis_index("tm")
    b = lax.axis_index("freq")
    t_in = visibilities.shape[2]
    f_blk = visibilities.shape[3]
    t_out = flag_mask.shape[0]
    channels = flag_mask.shape[1]

    taps_kept = masked_taps(fringe_taps, tap_windows)
    class_starts = jnp.cumsum(class_counts) - class_counts

    padded = extended(visibilities, (("tm", 2),), REACH)
    padded = jnp.pad(padded, ((0, 0), (0, SLOTS), (0, 0), (0, 0)))

    panel = lax.all_gather(filter_panels[0], "freq", axis=0, tiled=True)
    if q == 1:
        shift = ((a + 1) % nf) * f_blk
        panel = jnp.concatenate([panel, panel], axis=1)
        panel = lax.dynamic_slice_in_dim(panel, shift, channels, axis=1)

    c_own = a
    u_src = (a % q) * nf + b
    fit = None
    for r in range(nt):
        c_send = (u_src + r) % nt
        start = class_starts[c_send]
        rows = lax.optimization_barrier(lax.dynamic_slice_in_dim(padded, start, SLOTS, axis=1))
        taps = lax.dynamic_index_in_dim(taps_kept, c_send, axis=1, keepdims=False)
        chunk = convolve_class(rows, taps, class_counts[c_send], t_in)
        perm = []
        for sa in range(nt):
            for sb in range(nf):
                u = (sa % q) * nf + sb
                dc = (u + r) % nt
                perm.append((sa * nf + sb, dc * nf + sa // q))
        got = lax.ppermute(chunk, ("tm", "freq"), perm)
        u_dst = (c_own - r) % nt
        t_sub = u_dst // nf
        b_src = u_dst % nf
        if q == 1:
            gate = lax.dynamic_slice_in_dim(flag_mask, b_src * f_blk, f_blk, axis=1)
            cols = lax.slice_in_dim(panel, (nf - 1 - r) * f_blk, (nf - r) * f_blk, axis=1)
        else:
            gate = lax.dynamic_slice(flag_mask, (t_sub * t_in, b_src * f_blk), (t_in, f_blk))
            cols = lax.dynamic_slice_in_dim(panel, b_src * f_blk, f_blk, axis=1)
        weighted = got * gate.astype(jnp.bfloat16)
        part = jnp.einsum("rstj,ij->rsti", weighted, cols, preferred_element_type=jnp.float32)
        if fit is None:
            slotted = jnp.zeros((2, SLOTS, t_out, channels), jnp.bfloat16)
        if q == 1:
            fit = part if fit is None else fit + part
            slotted = lax.dynamic_update_slice_in_dim(slotted, got, b_src * f_blk, axis=3)
        else:
            if fit is None:
                fit = jnp.zeros((2, SLOTS, t_out, channels), jnp.float32)
            prev = lax.dynamic_slice_in_dim(fit, t_sub * t_in, t_in, axis=2)
            fit = lax.dynamic_update_slice_in_dim(fit, prev + part, t_sub * t_in, axis=2)
            slotted = lax.dynamic_update_slice(slotted, got, (0, 0, t_sub * t_in, b_src * f_blk))
    cleaned = (slotted.astype(jnp.float32) - fit).astype(jnp.bfloat16)
    return cleaned[:, None]


def solution(mesh):
    return jax.shard_map(
        shards,
        mesh=mesh,
        in_specs=(
            P(None, "grp", "tm", "freq"),
            P("grp"),
            P("grp"),
            P("grp"),
            P(None, "grp", None),
            P("freq", None),
            P(("grp", "tm"), "freq", None),
        ),
        out_specs=P(None, ("grp", "tm"), None, "freq", None),
        check_vma=False,
    )
```

```python
import jax
import jax.numpy as jnp
from jax import lax
from jax.sharding import PartitionSpec as P


SLOTS = 32
REACH = 4


def extended(cells, sides, width):
    for axis, dim in sides:
        count = lax.axis_size(axis)
        ends = count - 1
        head = lax.slice_in_dim(cells, 0, width, axis=dim)
        tail = lax.slice_in_dim(cells, cells.shape[dim] - width, cells.shape[dim], axis=dim)
        cells = jnp.concatenate(
            [
                lax.ppermute(tail, axis, [(i, (i + 1) % count) for i in range(ends)]),
                cells,
                lax.ppermute(head, axis, [((i + 1) % count, i) for i in range(ends)]),
            ],
            axis=dim,
        )
    return cells


def masked_taps(fringe_taps, tap_windows):
    offsets = jnp.abs(jnp.arange(2 * REACH + 1, dtype=jnp.int32) - REACH)
    keep = (offsets[None, :] <= tap_windows[:, None]).astype(jnp.float32)
    return fringe_taps * keep[None, :, :]


def convolve(rows, slot_taps, length):
    real_part = jnp.zeros(rows.shape[1:2] + (length,) + rows.shape[3:], jnp.float32)
    imag_part = jnp.zeros_like(real_part)
    for offset in range(2 * REACH + 1):
        shifted = lax.slice_in_dim(rows, 2 * REACH - offset, 2 * REACH - offset + length, axis=2)
        tap_real = slot_taps[0, :, offset][:, None, None]
        tap_imag = slot_taps[1, :, offset][:, None, None]
        real_part = real_part + tap_real * shifted[0] - tap_imag * shifted[1]
        imag_part = imag_part + tap_real * shifted[1] + tap_imag * shifted[0]
    return jnp.stack([real_part, imag_part]).astype(jnp.bfloat16)


def convolve_class(rows, taps, count, length):
    live = (jnp.arange(rows.shape[1], dtype=jnp.int32) < count).astype(jnp.float32)
    return convolve(rows, taps[:, None, :] * live[None, :, None], length)


def to_slots(per_baseline, class_counts):
    class_starts = jnp.cumsum(class_counts) - class_counts
    slot_positions = jnp.arange(SLOTS, dtype=jnp.int32)
    input_visibility = jnp.clip(
        class_starts[:, None] + slot_positions[None, :], 0, per_baseline.shape[1] - 1
    )
    live_slot = slot_positions[None, :] < class_counts[:, None]
    gathered = jnp.take(per_baseline, input_visibility.reshape(-1), axis=1)
    gathered = gathered.reshape(per_baseline.shape[:1] + live_slot.shape + per_baseline.shape[2:])
    return jnp.where(live_slot[None, :, :, None, None], gathered, jnp.zeros((), per_baseline.dtype))


def two_stage(
    visibilities, class_ids, class_counts, tap_windows, fringe_taps, flag_mask, filter_panels
):
    taps_kept = masked_taps(fringe_taps, tap_windows)
    padded = extended(visibilities, (("tm", 2),), REACH)
    row_taps = taps_kept[:, class_ids, :]
    filtered = convolve(padded, row_taps, visibilities.shape[2])
    slotted = to_slots(filtered, class_counts)
    local_block = lax.all_to_all(
        lax.all_to_all(slotted, "tm", split_axis=1, concat_axis=3, tiled=True),
        "freq",
        split_axis=3,
        concat_axis=4,
        tiled=True,
    )
    weighted = local_block * flag_mask.astype(jnp.bfloat16)
    dayenu_fit = jnp.einsum(
        "rcstj,cij->rcsti",
        weighted,
        lax.all_gather(filter_panels, "freq", axis=1, tiled=True),
        preferred_element_type=jnp.float32,
    )
    return (local_block.astype(jnp.float32) - dayenu_fit).astype(jnp.bfloat16)


def shards(
    visibilities, class_ids, class_counts, tap_windows, fringe_taps, flag_mask, filter_panels
):
    nt = lax.axis_size("tm")
    nf = lax.axis_size("freq")
    if nt != nf:
        return two_stage(
            visibilities, class_ids, class_counts, tap_windows, fringe_taps, flag_mask,
            filter_panels,
        )
    q = nt // nf
    a = lax.axis_index("tm")
    b = lax.axis_index("freq")
    t_in = visibilities.shape[2]
    f_blk = visibilities.shape[3]
    t_out = flag_mask.shape[0]
    channels = flag_mask.shape[1]

    taps_kept = masked_taps(fringe_taps, tap_windows)
    class_starts = jnp.cumsum(class_counts) - class_counts

    padded = extended(visibilities, (("tm", 2),), REACH)
    padded = jnp.pad(padded, ((0, 0), (0, SLOTS), (0, 0), (0, 0)))

    if q == 1 and nf & (nf - 1) == 0:
        blocks = filter_panels[0][None]
        step = nf // 2
        while step >= 1:
            perm = [(f, f ^ step) for f in range(nf)]
            blocks = jnp.concatenate([blocks, lax.ppermute(blocks, "freq", perm)], axis=0)
            step //= 2
        codes = [0]
        step = nf // 2
        while step >= 1:
            codes = codes + [x ^ step for x in codes]
            step //= 2
        where = {code: m for m, code in enumerate(codes)}
        rows = []
        for k in range(nf):
            pick = sum(
                jnp.where((k ^ b) == code, m, 0) for code, m in where.items()
            )
            rows.append(lax.dynamic_index_in_dim(blocks, pick, 0, keepdims=False))
        panel = jnp.concatenate(rows, axis=0)
    else:
        panel = lax.all_gather(filter_panels[0], "freq", axis=0, tiled=True)
    if q == 1:
        shift = ((a + 1) % nf) * f_blk
        panel = jnp.concatenate([panel, panel], axis=1)
        panel = lax.dynamic_slice_in_dim(panel, shift, channels, axis=1)

    c_own = a
    u_src = (a % q) * nf + b
    fit = None
    for r in range(nt):
        c_send = (u_src + r) % nt
        start = class_starts[c_send]
        rows = lax.optimization_barrier(lax.dynamic_slice_in_dim(padded, start, SLOTS, axis=1))
        taps = lax.dynamic_index_in_dim(taps_kept, c_send, axis=1, keepdims=False)
        chunk = convolve_class(rows, taps, class_counts[c_send], t_in)
        perm = []
        for sa in range(nt):
            for sb in range(nf):
                u = (sa % q) * nf + sb
                dc = (u + r) % nt
                perm.append((sa * nf + sb, dc * nf + sa // q))
        got = lax.ppermute(chunk, ("tm", "freq"), perm)
        u_dst = (c_own - r) % nt
        t_sub = u_dst // nf
        b_src = u_dst % nf
        if q == 1:
            gate = lax.dynamic_slice_in_dim(flag_mask, b_src * f_blk, f_blk, axis=1)
            cols = lax.slice_in_dim(panel, (nf - 1 - r) * f_blk, (nf - r) * f_blk, axis=1)
        else:
            gate = lax.dynamic_slice(flag_mask, (t_sub * t_in, b_src * f_blk), (t_in, f_blk))
            cols = lax.dynamic_slice_in_dim(panel, b_src * f_blk, f_blk, axis=1)
        weighted = got * gate.astype(jnp.bfloat16)
        part = jnp.einsum("rstj,ij->rsti", weighted, cols, preferred_element_type=jnp.float32)
        if fit is None:
            slotted = jnp.zeros((2, SLOTS, t_out, channels), jnp.bfloat16)
        if q == 1:
            fit = part if fit is None else fit + part
            slotted = lax.dynamic_update_slice_in_dim(slotted, got, b_src * f_blk, axis=3)
        else:
            if fit is None:
                fit = jnp.zeros((2, SLOTS, t_out, channels), jnp.float32)
            prev = lax.dynamic_slice_in_dim(fit, t_sub * t_in, t_in, axis=2)
            fit = lax.dynamic_update_slice_in_dim(fit, prev + part, t_sub * t_in, axis=2)
            slotted = lax.dynamic_update_slice(slotted, got, (0, 0, t_sub * t_in, b_src * f_blk))
    cleaned = (slotted.astype(jnp.float32) - fit).astype(jnp.bfloat16)
    return cleaned[:, None]


def solution(mesh):
    return jax.shard_map(
        shards,
        mesh=mesh,
        in_specs=(
            P(None, "grp", "tm", "freq"),
            P("grp"),
            P("grp"),
            P("grp"),
            P(None, "grp", None),
            P("freq", None),
            P(("grp", "tm"), "freq", None),
        ),
        out_specs=P(None, ("grp", "tm"), None, "freq", None),
        check_vma=False,
    )
```

```python
import functools

import jax
import jax.numpy as jnp
from jax import lax
from jax.sharding import PartitionSpec as P


SLOTS = 32
REACH = 4


def extended(cells, sides, width):
    for axis, dim in sides:
        count = lax.axis_size(axis)
        ends = count - 1
        head = lax.slice_in_dim(cells, 0, width, axis=dim)
        tail = lax.slice_in_dim(cells, cells.shape[dim] - width, cells.shape[dim], axis=dim)
        cells = jnp.concatenate(
            [
                lax.ppermute(tail, axis, [(i, (i + 1) % count) for i in range(ends)]),
                cells,
                lax.ppermute(head, axis, [((i + 1) % count, i) for i in range(ends)]),
            ],
            axis=dim,
        )
    return cells


def in_order(blocks, order):
    return jnp.concatenate([blocks[m] for m in order], axis=0)


def masked_taps(fringe_taps, tap_windows):
    offsets = jnp.abs(jnp.arange(2 * REACH + 1, dtype=jnp.int32) - REACH)
    keep = (offsets[None, :] <= tap_windows[:, None]).astype(jnp.float32)
    return fringe_taps * keep[None, :, :]


def convolve(rows, slot_taps, length):
    real_part = jnp.zeros(rows.shape[1:2] + (length,) + rows.shape[3:], jnp.float32)
    imag_part = jnp.zeros_like(real_part)
    for offset in range(2 * REACH + 1):
        shifted = lax.slice_in_dim(rows, 2 * REACH - offset, 2 * REACH - offset + length, axis=2)
        tap_real = slot_taps[0, :, offset][:, None, None]
        tap_imag = slot_taps[1, :, offset][:, None, None]
        real_part = real_part + tap_real * shifted[0] - tap_imag * shifted[1]
        imag_part = imag_part + tap_real * shifted[1] + tap_imag * shifted[0]
    return jnp.stack([real_part, imag_part]).astype(jnp.bfloat16)


def convolve_class(rows, taps, count, length):
    live = (jnp.arange(rows.shape[1], dtype=jnp.int32) < count).astype(jnp.float32)
    return convolve(rows, taps[:, None, :] * live[None, :, None], length)


def to_slots(per_baseline, class_counts):
    class_starts = jnp.cumsum(class_counts) - class_counts
    slot_positions = jnp.arange(SLOTS, dtype=jnp.int32)
    input_visibility = jnp.clip(
        class_starts[:, None] + slot_positions[None, :], 0, per_baseline.shape[1] - 1
    )
    live_slot = slot_positions[None, :] < class_counts[:, None]
    gathered = jnp.take(per_baseline, input_visibility.reshape(-1), axis=1)
    gathered = gathered.reshape(per_baseline.shape[:1] + live_slot.shape + per_baseline.shape[2:])
    return jnp.where(live_slot[None, :, :, None, None], gathered, jnp.zeros((), per_baseline.dtype))


def two_stage(
    visibilities, class_ids, class_counts, tap_windows, fringe_taps, flag_mask, filter_panels
):
    taps_kept = masked_taps(fringe_taps, tap_windows)
    padded = extended(visibilities, (("tm", 2),), REACH)
    row_taps = taps_kept[:, class_ids, :]
    filtered = convolve(padded, row_taps, visibilities.shape[2])
    slotted = to_slots(filtered, class_counts)
    local_block = lax.all_to_all(
        lax.all_to_all(slotted, "tm", split_axis=1, concat_axis=3, tiled=True),
        "freq",
        split_axis=3,
        concat_axis=4,
        tiled=True,
    )
    weighted = local_block * flag_mask.astype(jnp.bfloat16)
    dayenu_fit = jnp.einsum(
        "rcstj,cij->rcsti",
        weighted,
        lax.all_gather(filter_panels, "freq", axis=1, tiled=True),
        preferred_element_type=jnp.float32,
    )
    return (local_block.astype(jnp.float32) - dayenu_fit).astype(jnp.bfloat16)


def shards(
    visibilities, class_ids, class_counts, tap_windows, fringe_taps, flag_mask, filter_panels
):
    nt = lax.axis_size("tm")
    nf = lax.axis_size("freq")
    if nt != nf:
        return two_stage(
            visibilities, class_ids, class_counts, tap_windows, fringe_taps, flag_mask,
            filter_panels,
        )
    q = nt // nf
    a = lax.axis_index("tm")
    b = lax.axis_index("freq")
    t_in = visibilities.shape[2]
    f_blk = visibilities.shape[3]
    t_out = flag_mask.shape[0]
    channels = flag_mask.shape[1]

    taps_kept = masked_taps(fringe_taps, tap_windows)
    class_starts = jnp.cumsum(class_counts) - class_counts

    padded = extended(visibilities, (("tm", 2),), REACH)
    padded = jnp.pad(padded, ((0, 0), (0, SLOTS), (0, 0), (0, 0)))

    if q == 1 and nf & (nf - 1) == 0:
        blocks = filter_panels[0][None]
        step = nf // 2
        while step >= 1:
            perm = [(f, f ^ step) for f in range(nf)]
            blocks = jnp.concatenate([blocks, lax.ppermute(blocks, "freq", perm)], axis=0)
            step //= 2
        codes = [0]
        step = nf // 2
        while step >= 1:
            codes = codes + [x ^ step for x in codes]
            step //= 2
        where = {code: m for m, code in enumerate(codes)}
        branches = [
            functools.partial(in_order, order=[where[k ^ own] for k in range(nf)])
            for own in range(nf)
        ]
        panel = lax.switch(b, branches, blocks)
    else:
        panel = lax.all_gather(filter_panels[0], "freq", axis=0, tiled=True)
    if q == 1:
        shift = ((a + 1) % nf) * f_blk
        panel = jnp.concatenate([panel, panel], axis=1)
        panel = lax.dynamic_slice_in_dim(panel, shift, channels, axis=1)

    c_own = a
    u_src = (a % q) * nf + b
    fit = None
    local = jnp.pad(visibilities, ((0, 0), (0, SLOTS), (0, 0), (0, 0)))
    inner = t_in - 2 * REACH
    for r in range(nt):
        c_send = (u_src + r) % nt
        start = class_starts[c_send]
        taps = lax.dynamic_index_in_dim(taps_kept, c_send, axis=1, keepdims=False)
        count = class_counts[c_send]
        perm = []
        for sa in range(nt):
            for sb in range(nf):
                u = (sa % q) * nf + sb
                dc = (u + r) % nt
                perm.append((sa * nf + sb, dc * nf + sa // q))
        if inner > 0:
            own = lax.optimization_barrier(lax.dynamic_slice_in_dim(local, start, SLOTS, axis=1))
            middle = convolve_class(own, taps, count, inner)
            got_mid = lax.ppermute(middle, ("tm", "freq"), perm)
        rows = lax.optimization_barrier(lax.dynamic_slice_in_dim(padded, start, SLOTS, axis=1))
        if inner > 0:
            head = convolve_class(rows[:, :, : 3 * REACH], taps, count, REACH)
            tail = convolve_class(rows[:, :, t_in - REACH :], taps, count, REACH)
            chunk = jnp.concatenate([head, tail], axis=2)
        else:
            chunk = convolve_class(rows, taps, count, t_in)
        got = lax.ppermute(chunk, ("tm", "freq"), perm)
        if inner > 0:
            got = jnp.concatenate([got[:, :, :REACH], got_mid, got[:, :, REACH:]], axis=2)
        u_dst = (c_own - r) % nt
        t_sub = u_dst // nf
        b_src = u_dst % nf
        if q == 1:
            gate = lax.dynamic_slice_in_dim(flag_mask, b_src * f_blk, f_blk, axis=1)
            cols = lax.slice_in_dim(panel, (nf - 1 - r) * f_blk, (nf - r) * f_blk, axis=1)
        else:
            gate = lax.dynamic_slice(flag_mask, (t_sub * t_in, b_src * f_blk), (t_in, f_blk))
            cols = lax.dynamic_slice_in_dim(panel, b_src * f_blk, f_blk, axis=1)
        weighted = got * gate.astype(jnp.bfloat16)
        part = jnp.einsum("rstj,ij->rsti", weighted, cols, preferred_element_type=jnp.float32)
        if fit is None:
            slotted = jnp.zeros((2, SLOTS, t_out, channels), jnp.bfloat16)
        if q == 1:
            fit = part if fit is None else fit + part
            slotted = lax.dynamic_update_slice_in_dim(slotted, got, b_src * f_blk, axis=3)
        else:
            if fit is None:
                fit = jnp.zeros((2, SLOTS, t_out, channels), jnp.float32)
            prev = lax.dynamic_slice_in_dim(fit, t_sub * t_in, t_in, axis=2)
            fit = lax.dynamic_update_slice_in_dim(fit, prev + part, t_sub * t_in, axis=2)
            slotted = lax.dynamic_update_slice(slotted, got, (0, 0, t_sub * t_in, b_src * f_blk))
    cleaned = (slotted.astype(jnp.float32) - fit).astype(jnp.bfloat16)
    return cleaned[:, None]


def solution(mesh):
    return jax.shard_map(
        shards,
        mesh=mesh,
        in_specs=(
            P(None, "grp", "tm", "freq"),
            P("grp"),
            P("grp"),
            P("grp"),
            P(None, "grp", None),
            P("freq", None),
            P(("grp", "tm"), "freq", None),
        ),
        out_specs=P(None, ("grp", "tm"), None, "freq", None),
        check_vma=False,
    )
```

```python
import functools

import jax
import jax.numpy as jnp
from jax import lax
from jax.sharding import PartitionSpec as P


SLOTS = 32
REACH = 4


def extended(cells, sides, width):
    for axis, dim in sides:
        count = lax.axis_size(axis)
        ends = count - 1
        head = lax.slice_in_dim(cells, 0, width, axis=dim)
        tail = lax.slice_in_dim(cells, cells.shape[dim] - width, cells.shape[dim], axis=dim)
        cells = jnp.concatenate(
            [
                lax.ppermute(tail, axis, [(i, (i + 1) % count) for i in range(ends)]),
                cells,
                lax.ppermute(head, axis, [((i + 1) % count, i) for i in range(ends)]),
            ],
            axis=dim,
        )
    return cells


def in_order(blocks, order):
    return jnp.concatenate([blocks[m] for m in order], axis=0)


def masked_taps(fringe_taps, tap_windows):
    offsets = jnp.abs(jnp.arange(2 * REACH + 1, dtype=jnp.int32) - REACH)
    keep = (offsets[None, :] <= tap_windows[:, None]).astype(jnp.float32)
    return fringe_taps * keep[None, :, :]


def convolve(rows, slot_taps, length):
    real_part = jnp.zeros(rows.shape[1:2] + (length,) + rows.shape[3:], jnp.float32)
    imag_part = jnp.zeros_like(real_part)
    for offset in range(2 * REACH + 1):
        shifted = lax.slice_in_dim(rows, 2 * REACH - offset, 2 * REACH - offset + length, axis=2)
        tap_real = slot_taps[0, :, offset][:, None, None]
        tap_imag = slot_taps[1, :, offset][:, None, None]
        real_part = real_part + tap_real * shifted[0] - tap_imag * shifted[1]
        imag_part = imag_part + tap_real * shifted[1] + tap_imag * shifted[0]
    return jnp.stack([real_part, imag_part]).astype(jnp.bfloat16)


def to_slots(per_baseline, class_counts):
    class_starts = jnp.cumsum(class_counts) - class_counts
    slot_positions = jnp.arange(SLOTS, dtype=jnp.int32)
    input_visibility = jnp.clip(
        class_starts[:, None] + slot_positions[None, :], 0, per_baseline.shape[1] - 1
    )
    live_slot = slot_positions[None, :] < class_counts[:, None]
    gathered = jnp.take(per_baseline, input_visibility.reshape(-1), axis=1)
    gathered = gathered.reshape(per_baseline.shape[:1] + live_slot.shape + per_baseline.shape[2:])
    return jnp.where(live_slot[None, :, :, None, None], gathered, jnp.zeros((), per_baseline.dtype))


def two_stage(
    visibilities, class_ids, class_counts, tap_windows, fringe_taps, flag_mask, filter_panels
):
    taps_kept = masked_taps(fringe_taps, tap_windows)
    padded = extended(visibilities, (("tm", 2),), REACH)
    row_taps = taps_kept[:, class_ids, :]
    filtered = convolve(padded, row_taps, visibilities.shape[2])
    slotted = to_slots(filtered, class_counts)
    local_block = lax.all_to_all(
        lax.all_to_all(slotted, "tm", split_axis=1, concat_axis=3, tiled=True),
        "freq",
        split_axis=3,
        concat_axis=4,
        tiled=True,
    )
    weighted = local_block * flag_mask.astype(jnp.bfloat16)
    dayenu_fit = jnp.einsum(
        "rcstj,cij->rcsti",
        weighted,
        lax.all_gather(filter_panels, "freq", axis=1, tiled=True),
        preferred_element_type=jnp.float32,
    )
    return (local_block.astype(jnp.float32) - dayenu_fit).astype(jnp.bfloat16)


def shards(
    visibilities, class_ids, class_counts, tap_windows, fringe_taps, flag_mask, filter_panels
):
    nt = lax.axis_size("tm")
    nf = lax.axis_size("freq")
    if nt != nf:
        return two_stage(
            visibilities, class_ids, class_counts, tap_windows, fringe_taps, flag_mask,
            filter_panels,
        )
    a = lax.axis_index("tm")
    b = lax.axis_index("freq")
    t_in = visibilities.shape[2]
    f_blk = visibilities.shape[3]
    t_out = flag_mask.shape[0]
    channels = flag_mask.shape[1]

    taps_kept = masked_taps(fringe_taps, tap_windows)
    class_starts = jnp.cumsum(class_counts) - class_counts

    padded = extended(visibilities, (("tm", 2),), REACH)
    padded = jnp.pad(padded, ((0, 0), (0, SLOTS), (0, 0), (0, 0)))

    if nf & (nf - 1) == 0:
        blocks = filter_panels[0][None]
        step = nf // 2
        while step >= 1:
            perm = [(f, f ^ step) for f in range(nf)]
            blocks = jnp.concatenate([blocks, lax.ppermute(blocks, "freq", perm)], axis=0)
            step //= 2
        codes = [0]
        step = nf // 2
        while step >= 1:
            codes = codes + [x ^ step for x in codes]
            step //= 2
        where = {code: m for m, code in enumerate(codes)}
        branches = [
            functools.partial(in_order, order=[where[k ^ own] for k in range(nf)])
            for own in range(nf)
        ]
        panel = lax.switch(b, branches, blocks)
    else:
        panel = lax.all_gather(filter_panels[0], "freq", axis=0, tiled=True)
    shift = lax.rem(a + 1, nf) * f_blk
    panel = jnp.concatenate([panel, panel], axis=1)
    panel = lax.dynamic_slice_in_dim(panel, shift, channels, axis=1)

    rounds = jnp.arange(nt, dtype=jnp.int32)
    c_all = lax.rem(b + rounds, nt)
    start_all = jnp.take(class_starts, c_all)
    count_all = jnp.take(class_counts, c_all)
    live_all = (jnp.arange(SLOTS, dtype=jnp.int32)[None, :] < count_all[:, None]).astype(jnp.float32)
    taps_all = jnp.take(taps_kept, c_all, axis=1)[:, :, None, :] * live_all[None, :, :, None]
    offset_all = lax.rem(a + nt - rounds, nt) * f_blk
    fit = None
    slotted = jnp.zeros((2, SLOTS, t_out, channels), jnp.bfloat16)
    for r in range(nt):
        rows = lax.optimization_barrier(
            lax.dynamic_slice_in_dim(padded, start_all[r], SLOTS, axis=1)
        )
        chunk = convolve(rows, taps_all[:, r], t_in)
        perm = []
        for sa in range(nt):
            for sb in range(nf):
                perm.append((sa * nf + sb, ((sb + r) % nt) * nf + sa))
        got = lax.ppermute(chunk, ("tm", "freq"), perm)
        b_off = offset_all[r]
        gate = lax.dynamic_slice_in_dim(flag_mask, b_off, f_blk, axis=1)
        cols = lax.slice_in_dim(panel, (nf - 1 - r) * f_blk, (nf - r) * f_blk, axis=1)
        weighted = got * gate.astype(jnp.bfloat16)
        part = jnp.einsum("rstj,ij->rsti", weighted, cols, preferred_element_type=jnp.float32)
        fit = part if fit is None else fit + part
        slotted = lax.dynamic_update_slice_in_dim(slotted, got, b_off, axis=3)
    cleaned = (slotted.astype(jnp.float32) - fit).astype(jnp.bfloat16)
    return cleaned[:, None]


def solution(mesh):
    return jax.shard_map(
        shards,
        mesh=mesh,
        in_specs=(
            P(None, "grp", "tm", "freq"),
            P("grp"),
            P("grp"),
            P("grp"),
            P(None, "grp", None),
            P("freq", None),
            P(("grp", "tm"), "freq", None),
        ),
        out_specs=P(None, ("grp", "tm"), None, "freq", None),
        check_vma=False,
    )
```

```python
import functools

import jax
import jax.numpy as jnp
from jax import lax
from jax.sharding import PartitionSpec as P


SLOTS = 32
REACH = 4


def extended(cells, sides, width):
    for axis, dim in sides:
        count = lax.axis_size(axis)
        ends = count - 1
        head = lax.slice_in_dim(cells, 0, width, axis=dim)
        tail = lax.slice_in_dim(cells, cells.shape[dim] - width, cells.shape[dim], axis=dim)
        cells = jnp.concatenate(
            [
                lax.ppermute(tail, axis, [(i, (i + 1) % count) for i in range(ends)]),
                cells,
                lax.ppermute(head, axis, [((i + 1) % count, i) for i in range(ends)]),
            ],
            axis=dim,
        )
    return cells


def in_order(blocks, order):
    return jnp.concatenate([blocks[m] for m in order], axis=0)


def masked_taps(fringe_taps, tap_windows):
    offsets = jnp.abs(jnp.arange(2 * REACH + 1, dtype=jnp.int32) - REACH)
    keep = (offsets[None, :] <= tap_windows[:, None]).astype(jnp.float32)
    return fringe_taps * keep[None, :, :]


def convolve(rows, slot_taps, length):
    real_part = jnp.zeros(rows.shape[1:2] + (length,) + rows.shape[3:], jnp.float32)
    imag_part = jnp.zeros_like(real_part)
    for offset in range(2 * REACH + 1):
        shifted = lax.slice_in_dim(rows, 2 * REACH - offset, 2 * REACH - offset + length, axis=2)
        tap_real = slot_taps[0, :, offset][:, None, None]
        tap_imag = slot_taps[1, :, offset][:, None, None]
        real_part = real_part + tap_real * shifted[0] - tap_imag * shifted[1]
        imag_part = imag_part + tap_real * shifted[1] + tap_imag * shifted[0]
    return jnp.stack([real_part, imag_part]).astype(jnp.bfloat16)


def convolve_class(rows, taps, count, length):
    live = (jnp.arange(rows.shape[1], dtype=jnp.int32) < count).astype(jnp.float32)
    return convolve(rows, taps[:, None, :] * live[None, :, None], length)


def to_slots(per_baseline, class_counts):
    class_starts = jnp.cumsum(class_counts) - class_counts
    slot_positions = jnp.arange(SLOTS, dtype=jnp.int32)
    input_visibility = jnp.clip(
        class_starts[:, None] + slot_positions[None, :], 0, per_baseline.shape[1] - 1
    )
    live_slot = slot_positions[None, :] < class_counts[:, None]
    gathered = jnp.take(per_baseline, input_visibility.reshape(-1), axis=1)
    gathered = gathered.reshape(per_baseline.shape[:1] + live_slot.shape + per_baseline.shape[2:])
    return jnp.where(live_slot[None, :, :, None, None], gathered, jnp.zeros((), per_baseline.dtype))


def two_stage(
    visibilities, class_ids, class_counts, tap_windows, fringe_taps, flag_mask, filter_panels
):
    taps_kept = masked_taps(fringe_taps, tap_windows)
    padded = extended(visibilities, (("tm", 2),), REACH)
    row_taps = taps_kept[:, class_ids, :]
    filtered = convolve(padded, row_taps, visibilities.shape[2])
    slotted = to_slots(filtered, class_counts)
    local_block = lax.all_to_all(
        lax.all_to_all(slotted, "tm", split_axis=1, concat_axis=3, tiled=True),
        "freq",
        split_axis=3,
        concat_axis=4,
        tiled=True,
    )
    weighted = local_block * flag_mask.astype(jnp.bfloat16)
    dayenu_fit = jnp.einsum(
        "rcstj,cij->rcsti",
        weighted,
        lax.all_gather(filter_panels, "freq", axis=1, tiled=True),
        preferred_element_type=jnp.float32,
    )
    return (local_block.astype(jnp.float32) - dayenu_fit).astype(jnp.bfloat16)


def shards(
    visibilities, class_ids, class_counts, tap_windows, fringe_taps, flag_mask, filter_panels
):
    nt = lax.axis_size("tm")
    nf = lax.axis_size("freq")
    if nt != nf:
        return two_stage(
            visibilities, class_ids, class_counts, tap_windows, fringe_taps, flag_mask,
            filter_panels,
        )
    q = nt // nf
    a = lax.axis_index("tm")
    b = lax.axis_index("freq")
    t_in = visibilities.shape[2]
    f_blk = visibilities.shape[3]
    t_out = flag_mask.shape[0]
    channels = flag_mask.shape[1]

    taps_kept = masked_taps(fringe_taps, tap_windows)
    class_starts = jnp.cumsum(class_counts) - class_counts

    padded = extended(visibilities, (("tm", 2),), REACH)
    inner = t_in - 2 * REACH
    if inner > 0:
        pad_b = ((0, 0), (0, SLOTS), (0, 0), (0, 0))
        local = jnp.pad(visibilities, pad_b)
        head_src = jnp.pad(lax.slice_in_dim(padded, 0, 3 * REACH, axis=2), pad_b)
        tail_src = jnp.pad(lax.slice_in_dim(padded, t_in - REACH, t_in + 2 * REACH, axis=2), pad_b)
    else:
        padded = jnp.pad(padded, ((0, 0), (0, SLOTS), (0, 0), (0, 0)))

    if q == 1 and nf & (nf - 1) == 0:
        blocks = filter_panels[0][None]
        step = nf // 2
        while step >= 1:
            perm = [(f, f ^ step) for f in range(nf)]
            blocks = jnp.concatenate([blocks, lax.ppermute(blocks, "freq", perm)], axis=0)
            step //= 2
        codes = [0]
        step = nf // 2
        while step >= 1:
            codes = codes + [x ^ step for x in codes]
            step //= 2
        where = {code: m for m, code in enumerate(codes)}
        branches = [
            functools.partial(in_order, order=[where[k ^ own] for k in range(nf)])
            for own in range(nf)
        ]
        panel = lax.switch(b, branches, blocks)
    else:
        panel = lax.all_gather(filter_panels[0], "freq", axis=0, tiled=True)
    if q == 1:
        shift = ((a + 1) % nf) * f_blk
        panel = jnp.concatenate([panel, panel], axis=1)
        panel = lax.dynamic_slice_in_dim(panel, shift, channels, axis=1)

    c_own = a
    u_src = (a % q) * nf + b
    fit = None
    for r in range(nt):
        c_send = (u_src + r) % nt
        start = class_starts[c_send]
        taps = lax.dynamic_index_in_dim(taps_kept, c_send, axis=1, keepdims=False)
        count = class_counts[c_send]
        if inner > 0:
            own = lax.dynamic_slice_in_dim(local, start, SLOTS, axis=1)
            middle = convolve_class(own, taps, count, inner)
            head = convolve_class(lax.dynamic_slice_in_dim(head_src, start, SLOTS, axis=1), taps, count, REACH)
            tail = convolve_class(lax.dynamic_slice_in_dim(tail_src, start, SLOTS, axis=1), taps, count, REACH)
            chunk = jnp.concatenate([head, middle, tail], axis=2)
        else:
            rows = lax.optimization_barrier(lax.dynamic_slice_in_dim(padded, start, SLOTS, axis=1))
            chunk = convolve_class(rows, taps, count, t_in)
        perm = []
        for sa in range(nt):
            for sb in range(nf):
                u = (sa % q) * nf + sb
                dc = (u + r) % nt
                perm.append((sa * nf + sb, dc * nf + sa // q))
        got = lax.ppermute(chunk, ("tm", "freq"), perm)
        u_dst = (c_own - r) % nt
        t_sub = u_dst // nf
        b_src = u_dst % nf
        if q == 1:
            gate = lax.dynamic_slice_in_dim(flag_mask, b_src * f_blk, f_blk, axis=1)
            cols = lax.slice_in_dim(panel, (nf - 1 - r) * f_blk, (nf - r) * f_blk, axis=1)
        else:
            gate = lax.dynamic_slice(flag_mask, (t_sub * t_in, b_src * f_blk), (t_in, f_blk))
            cols = lax.dynamic_slice_in_dim(panel, b_src * f_blk, f_blk, axis=1)
        weighted = got * gate.astype(jnp.bfloat16)
        part = jnp.einsum("rstj,ij->rsti", weighted, cols, preferred_element_type=jnp.float32)
        if fit is None:
            slotted = jnp.zeros((2, SLOTS, t_out, channels), jnp.bfloat16)
        if q == 1:
            fit = part if fit is None else fit + part
            slotted = lax.dynamic_update_slice_in_dim(slotted, got, b_src * f_blk, axis=3)
        else:
            if fit is None:
                fit = jnp.zeros((2, SLOTS, t_out, channels), jnp.float32)
            prev = lax.dynamic_slice_in_dim(fit, t_sub * t_in, t_in, axis=2)
            fit = lax.dynamic_update_slice_in_dim(fit, prev + part, t_sub * t_in, axis=2)
            slotted = lax.dynamic_update_slice(slotted, got, (0, 0, t_sub * t_in, b_src * f_blk))
    cleaned = (slotted.astype(jnp.float32) - fit).astype(jnp.bfloat16)
    return cleaned[:, None]


def solution(mesh):
    return jax.shard_map(
        shards,
        mesh=mesh,
        in_specs=(
            P(None, "grp", "tm", "freq"),
            P("grp"),
            P("grp"),
            P("grp"),
            P(None, "grp", None),
            P("freq", None),
            P(("grp", "tm"), "freq", None),
        ),
        out_specs=P(None, ("grp", "tm"), None, "freq", None),
        check_vma=False,
    )
```

```python
import functools

import jax
import jax.numpy as jnp
from jax import lax
from jax.sharding import PartitionSpec as P


SLOTS = 32
REACH = 4


def extended(cells, sides, width):
    for axis, dim in sides:
        count = lax.axis_size(axis)
        ends = count - 1
        head = lax.slice_in_dim(cells, 0, width, axis=dim)
        tail = lax.slice_in_dim(cells, cells.shape[dim] - width, cells.shape[dim], axis=dim)
        cells = jnp.concatenate(
            [
                lax.ppermute(tail, axis, [(i, (i + 1) % count) for i in range(ends)]),
                cells,
                lax.ppermute(head, axis, [((i + 1) % count, i) for i in range(ends)]),
            ],
            axis=dim,
        )
    return cells


def in_order(blocks, order):
    return jnp.concatenate([blocks[m] for m in order], axis=0)


def masked_taps(fringe_taps, tap_windows):
    offsets = jnp.abs(jnp.arange(2 * REACH + 1, dtype=jnp.int32) - REACH)
    keep = (offsets[None, :] <= tap_windows[:, None]).astype(jnp.float32)
    return fringe_taps * keep[None, :, :]


def convolve(rows, slot_taps, length):
    real_part = jnp.zeros(rows.shape[1:2] + (length,) + rows.shape[3:], jnp.float32)
    imag_part = jnp.zeros_like(real_part)
    for offset in range(2 * REACH + 1):
        shifted = lax.slice_in_dim(rows, 2 * REACH - offset, 2 * REACH - offset + length, axis=2)
        tap_real = slot_taps[0, :, offset][:, None, None]
        tap_imag = slot_taps[1, :, offset][:, None, None]
        real_part = real_part + tap_real * shifted[0] - tap_imag * shifted[1]
        imag_part = imag_part + tap_real * shifted[1] + tap_imag * shifted[0]
    return jnp.stack([real_part, imag_part]).astype(jnp.bfloat16)


def convolve_class(rows, taps, count, length):
    live = (jnp.arange(rows.shape[1], dtype=jnp.int32) < count).astype(jnp.float32)
    return convolve(rows, taps[:, None, :] * live[None, :, None], length)


def to_slots(per_baseline, class_counts):
    class_starts = jnp.cumsum(class_counts) - class_counts
    slot_positions = jnp.arange(SLOTS, dtype=jnp.int32)
    input_visibility = jnp.clip(
        class_starts[:, None] + slot_positions[None, :], 0, per_baseline.shape[1] - 1
    )
    live_slot = slot_positions[None, :] < class_counts[:, None]
    gathered = jnp.take(per_baseline, input_visibility.reshape(-1), axis=1)
    gathered = gathered.reshape(per_baseline.shape[:1] + live_slot.shape + per_baseline.shape[2:])
    return jnp.where(live_slot[None, :, :, None, None], gathered, jnp.zeros((), per_baseline.dtype))


def two_stage(
    visibilities, class_ids, class_counts, tap_windows, fringe_taps, flag_mask, filter_panels
):
    taps_kept = masked_taps(fringe_taps, tap_windows)
    padded = extended(visibilities, (("tm", 2),), REACH)
    row_taps = taps_kept[:, class_ids, :]
    filtered = convolve(padded, row_taps, visibilities.shape[2])
    slotted = to_slots(filtered, class_counts)
    local_block = lax.all_to_all(
        lax.all_to_all(slotted, "tm", split_axis=1, concat_axis=3, tiled=True),
        "freq",
        split_axis=3,
        concat_axis=4,
        tiled=True,
    )
    weighted = local_block * flag_mask.astype(jnp.bfloat16)
    dayenu_fit = jnp.einsum(
        "rcstj,cij->rcsti",
        weighted,
        lax.all_gather(filter_panels, "freq", axis=1, tiled=True),
        preferred_element_type=jnp.float32,
    )
    return (local_block.astype(jnp.float32) - dayenu_fit).astype(jnp.bfloat16)


def shards(
    visibilities, class_ids, class_counts, tap_windows, fringe_taps, flag_mask, filter_panels
):
    nt = lax.axis_size("tm")
    nf = lax.axis_size("freq")
    if nt != nf:
        return two_stage(
            visibilities, class_ids, class_counts, tap_windows, fringe_taps, flag_mask,
            filter_panels,
        )
    q = nt // nf
    a = lax.axis_index("tm")
    b = lax.axis_index("freq")
    t_in = visibilities.shape[2]
    f_blk = visibilities.shape[3]
    t_out = flag_mask.shape[0]
    channels = flag_mask.shape[1]

    taps_kept = masked_taps(fringe_taps, tap_windows)
    class_starts = jnp.cumsum(class_counts) - class_counts

    pad_b = ((0, 0), (0, SLOTS), (0, 0), (0, 0))
    local = jnp.pad(visibilities, pad_b)
    padded = extended(visibilities, (("tm", 2),), REACH)
    inner = t_in - 2 * REACH
    if inner > 0:
        head_src = jnp.pad(lax.slice_in_dim(padded, 0, 3 * REACH, axis=2), pad_b)
        tail_src = jnp.pad(lax.slice_in_dim(padded, t_in - REACH, t_in + 2 * REACH, axis=2), pad_b)
    padded = jnp.pad(padded, pad_b)

    if q == 1 and nf & (nf - 1) == 0:
        blocks = filter_panels[0][None]
        step = nf // 2
        while step >= 1:
            perm = [(f, f ^ step) for f in range(nf)]
            blocks = jnp.concatenate([blocks, lax.ppermute(blocks, "freq", perm)], axis=0)
            step //= 2
        codes = [0]
        step = nf // 2
        while step >= 1:
            codes = codes + [x ^ step for x in codes]
            step //= 2
        where = {code: m for m, code in enumerate(codes)}
        branches = [
            functools.partial(in_order, order=[where[k ^ own] for k in range(nf)])
            for own in range(nf)
        ]
        panel = lax.switch(b, branches, blocks)
    else:
        panel = lax.all_gather(filter_panels[0], "freq", axis=0, tiled=True)
    if q == 1:
        shift = ((a + 1) % nf) * f_blk
        panel = jnp.concatenate([panel, panel], axis=1)
        panel = lax.dynamic_slice_in_dim(panel, shift, channels, axis=1)

    c_own = a
    u_src = (a % q) * nf + b
    fit = None
    for r in range(nt):
        c_send = (u_src + r) % nt
        start = class_starts[c_send]
        taps = lax.dynamic_index_in_dim(taps_kept, c_send, axis=1, keepdims=False)
        count = class_counts[c_send]
        perm = []
        for sa in range(nt):
            for sb in range(nf):
                u = (sa % q) * nf + sb
                dc = (u + r) % nt
                perm.append((sa * nf + sb, dc * nf + sa // q))
        if r == 0 and inner > 0:
            own = lax.optimization_barrier(lax.dynamic_slice_in_dim(local, start, SLOTS, axis=1))
            middle = convolve_class(own, taps, count, inner)
            got_mid = lax.ppermute(middle, ("tm", "freq"), perm)
            head = convolve_class(lax.dynamic_slice_in_dim(head_src, start, SLOTS, axis=1), taps, count, REACH)
            tail = convolve_class(lax.dynamic_slice_in_dim(tail_src, start, SLOTS, axis=1), taps, count, REACH)
            got = lax.ppermute(jnp.concatenate([head, tail], axis=2), ("tm", "freq"), perm)
            got = jnp.concatenate([got[:, :, :REACH], got_mid, got[:, :, REACH:]], axis=2)
        else:
            rows = lax.optimization_barrier(lax.dynamic_slice_in_dim(padded, start, SLOTS, axis=1))
            chunk = convolve_class(rows, taps, count, t_in)
            got = lax.ppermute(chunk, ("tm", "freq"), perm)
        u_dst = (c_own - r) % nt
        t_sub = u_dst // nf
        b_src = u_dst % nf
        if q == 1:
            gate = lax.dynamic_slice_in_dim(flag_mask, b_src * f_blk, f_blk, axis=1)
            cols = lax.slice_in_dim(panel, (nf - 1 - r) * f_blk, (nf - r) * f_blk, axis=1)
        else:
            gate = lax.dynamic_slice(flag_mask, (t_sub * t_in, b_src * f_blk), (t_in, f_blk))
            cols = lax.dynamic_slice_in_dim(panel, b_src * f_blk, f_blk, axis=1)
        weighted = got * gate.astype(jnp.bfloat16)
        part = jnp.einsum("rstj,ij->rsti", weighted, cols, preferred_element_type=jnp.float32)
        if fit is None:
            slotted = jnp.zeros((2, SLOTS, t_out, channels), jnp.bfloat16)
        if q == 1:
            fit = part if fit is None else fit + part
            slotted = lax.dynamic_update_slice_in_dim(slotted, got, b_src * f_blk, axis=3)
        else:
            if fit is None:
                fit = jnp.zeros((2, SLOTS, t_out, channels), jnp.float32)
            prev = lax.dynamic_slice_in_dim(fit, t_sub * t_in, t_in, axis=2)
            fit = lax.dynamic_update_slice_in_dim(fit, prev + part, t_sub * t_in, axis=2)
            slotted = lax.dynamic_update_slice(slotted, got, (0, 0, t_sub * t_in, b_src * f_blk))
    cleaned = (slotted.astype(jnp.float32) - fit).astype(jnp.bfloat16)
    return cleaned[:, None]


def solution(mesh):
    return jax.shard_map(
        shards,
        mesh=mesh,
        in_specs=(
            P(None, "grp", "tm", "freq"),
            P("grp"),
            P("grp"),
            P("grp"),
            P(None, "grp", None),
            P("freq", None),
            P(("grp", "tm"), "freq", None),
        ),
        out_specs=P(None, ("grp", "tm"), None, "freq", None),
        check_vma=False,
    )
```

```python
import functools

import jax
import jax.numpy as jnp
from jax import lax
from jax.sharding import PartitionSpec as P


SLOTS = 32
REACH = 4


def extended(cells, sides, width):
    for axis, dim in sides:
        count = lax.axis_size(axis)
        ends = count - 1
        head = lax.slice_in_dim(cells, 0, width, axis=dim)
        tail = lax.slice_in_dim(cells, cells.shape[dim] - width, cells.shape[dim], axis=dim)
        cells = jnp.concatenate(
            [
                lax.ppermute(tail, axis, [(i, (i + 1) % count) for i in range(ends)]),
                cells,
                lax.ppermute(head, axis, [((i + 1) % count, i) for i in range(ends)]),
            ],
            axis=dim,
        )
    return cells


def in_order(blocks, order):
    return jnp.concatenate([blocks[m] for m in order], axis=0)


def masked_taps(fringe_taps, tap_windows):
    offsets = jnp.abs(jnp.arange(2 * REACH + 1, dtype=jnp.int32) - REACH)
    keep = (offsets[None, :] <= tap_windows[:, None]).astype(jnp.float32)
    return fringe_taps * keep[None, :, :]


def convolve(rows, slot_taps, length):
    real_part = jnp.zeros(rows.shape[1:2] + (length,) + rows.shape[3:], jnp.float32)
    imag_part = jnp.zeros_like(real_part)
    for offset in range(2 * REACH + 1):
        shifted = lax.slice_in_dim(rows, 2 * REACH - offset, 2 * REACH - offset + length, axis=2)
        tap_real = slot_taps[0, :, offset][:, None, None]
        tap_imag = slot_taps[1, :, offset][:, None, None]
        real_part = real_part + tap_real * shifted[0] - tap_imag * shifted[1]
        imag_part = imag_part + tap_real * shifted[1] + tap_imag * shifted[0]
    return jnp.stack([real_part, imag_part]).astype(jnp.bfloat16)


def convolve_class(rows, taps, count, length):
    live = (jnp.arange(rows.shape[1], dtype=jnp.int32) < count).astype(jnp.float32)
    return convolve(rows, taps[:, None, :] * live[None, :, None], length)


def to_slots(per_baseline, class_counts):
    class_starts = jnp.cumsum(class_counts) - class_counts
    slot_positions = jnp.arange(SLOTS, dtype=jnp.int32)
    input_visibility = jnp.clip(
        class_starts[:, None] + slot_positions[None, :], 0, per_baseline.shape[1] - 1
    )
    live_slot = slot_positions[None, :] < class_counts[:, None]
    gathered = jnp.take(per_baseline, input_visibility.reshape(-1), axis=1)
    gathered = gathered.reshape(per_baseline.shape[:1] + live_slot.shape + per_baseline.shape[2:])
    return jnp.where(live_slot[None, :, :, None, None], gathered, jnp.zeros((), per_baseline.dtype))


def two_stage(
    visibilities, class_ids, class_counts, tap_windows, fringe_taps, flag_mask, filter_panels
):
    taps_kept = masked_taps(fringe_taps, tap_windows)
    padded = extended(visibilities, (("tm", 2),), REACH)
    row_taps = taps_kept[:, class_ids, :]
    filtered = convolve(padded, row_taps, visibilities.shape[2])
    slotted = to_slots(filtered, class_counts)
    local_block = lax.all_to_all(
        lax.all_to_all(slotted, "tm", split_axis=1, concat_axis=3, tiled=True),
        "freq",
        split_axis=3,
        concat_axis=4,
        tiled=True,
    )
    weighted = local_block * flag_mask.astype(jnp.bfloat16)
    dayenu_fit = jnp.einsum(
        "rcstj,cij->rcsti",
        weighted,
        lax.all_gather(filter_panels, "freq", axis=1, tiled=True),
        preferred_element_type=jnp.float32,
    )
    return (local_block.astype(jnp.float32) - dayenu_fit).astype(jnp.bfloat16)


def shards(
    visibilities, class_ids, class_counts, tap_windows, fringe_taps, flag_mask, filter_panels
):
    nt = lax.axis_size("tm")
    nf = lax.axis_size("freq")
    if nt != nf:
        return two_stage(
            visibilities, class_ids, class_counts, tap_windows, fringe_taps, flag_mask,
            filter_panels,
        )
    q = nt // nf
    a = lax.axis_index("tm")
    b = lax.axis_index("freq")
    t_in = visibilities.shape[2]
    f_blk = visibilities.shape[3]
    t_out = flag_mask.shape[0]
    channels = flag_mask.shape[1]

    taps_kept = masked_taps(fringe_taps, tap_windows)
    class_starts = jnp.cumsum(class_counts) - class_counts

    padded = extended(visibilities, (("tm", 2),), REACH)
    padded = jnp.pad(padded, ((0, 0), (0, SLOTS), (0, 0), (0, 0)))

    if q == 1 and nf & (nf - 1) == 0:
        blocks = filter_panels[0][None]
        step = nf // 2
        while step >= 1:
            perm = [(f, f ^ step) for f in range(nf)]
            blocks = jnp.concatenate([blocks, lax.ppermute(blocks, "freq", perm)], axis=0)
            step //= 2
        codes = [0]
        step = nf // 2
        while step >= 1:
            codes = codes + [x ^ step for x in codes]
            step //= 2
        where = {code: m for m, code in enumerate(codes)}
        branches = [
            functools.partial(in_order, order=[where[k ^ own] for k in range(nf)])
            for own in range(nf)
        ]
        panel = lax.switch(b, branches, blocks)
    else:
        panel = lax.all_gather(filter_panels[0], "freq", axis=0, tiled=True)
    c_own = a
    u_src = (a % q) * nf + b
    fit = None
    for r in list(range(1, nt)) + [0]:
        c_send = (u_src + r) % nt
        start = class_starts[c_send]
        rows = lax.optimization_barrier(lax.dynamic_slice_in_dim(padded, start, SLOTS, axis=1))
        taps = lax.dynamic_index_in_dim(taps_kept, c_send, axis=1, keepdims=False)
        chunk = convolve_class(rows, taps, class_counts[c_send], t_in)
        perm = []
        for sa in range(nt):
            for sb in range(nf):
                u = (sa % q) * nf + sb
                dc = (u + r) % nt
                perm.append((sa * nf + sb, dc * nf + sa // q))
        got = lax.ppermute(chunk, ("tm", "freq"), perm)
        u_dst = (c_own - r) % nt
        t_sub = u_dst // nf
        b_src = u_dst % nf
        if q == 1:
            gate = lax.dynamic_slice_in_dim(flag_mask, b_src * f_blk, f_blk, axis=1)
            cols = lax.dynamic_slice_in_dim(panel, b_src * f_blk, f_blk, axis=1)
        else:
            gate = lax.dynamic_slice(flag_mask, (t_sub * t_in, b_src * f_blk), (t_in, f_blk))
            cols = lax.dynamic_slice_in_dim(panel, b_src * f_blk, f_blk, axis=1)
        weighted = got * gate.astype(jnp.bfloat16)
        part = jnp.einsum("rstj,ij->rsti", weighted, cols, preferred_element_type=jnp.float32)
        if fit is None:
            slotted = jnp.zeros((2, SLOTS, t_out, channels), jnp.bfloat16)
        if q == 1:
            fit = part if fit is None else fit + part
            slotted = lax.dynamic_update_slice_in_dim(slotted, got, b_src * f_blk, axis=3)
        else:
            if fit is None:
                fit = jnp.zeros((2, SLOTS, t_out, channels), jnp.float32)
            prev = lax.dynamic_slice_in_dim(fit, t_sub * t_in, t_in, axis=2)
            fit = lax.dynamic_update_slice_in_dim(fit, prev + part, t_sub * t_in, axis=2)
            slotted = lax.dynamic_update_slice(slotted, got, (0, 0, t_sub * t_in, b_src * f_blk))
    cleaned = (slotted.astype(jnp.float32) - fit).astype(jnp.bfloat16)
    return cleaned[:, None]


def solution(mesh):
    return jax.shard_map(
        shards,
        mesh=mesh,
        in_specs=(
            P(None, "grp", "tm", "freq"),
            P("grp"),
            P("grp"),
            P("grp"),
            P(None, "grp", None),
            P("freq", None),
            P(("grp", "tm"), "freq", None),
        ),
        out_specs=P(None, ("grp", "tm"), None, "freq", None),
        check_vma=False,
    )
```

```python
import functools

import jax
import jax.numpy as jnp
from jax import lax
from jax.sharding import PartitionSpec as P


SLOTS = 32
REACH = 4


def extended(cells, sides, width):
    for axis, dim in sides:
        count = lax.axis_size(axis)
        ends = count - 1
        head = lax.slice_in_dim(cells, 0, width, axis=dim)
        tail = lax.slice_in_dim(cells, cells.shape[dim] - width, cells.shape[dim], axis=dim)
        cells = jnp.concatenate(
            [
                lax.ppermute(tail, axis, [(i, (i + 1) % count) for i in range(ends)]),
                cells,
                lax.ppermute(head, axis, [((i + 1) % count, i) for i in range(ends)]),
            ],
            axis=dim,
        )
    return cells


def in_order(blocks, order):
    return jnp.concatenate([blocks[m] for m in order], axis=0)


def masked_taps(fringe_taps, tap_windows):
    offsets = jnp.abs(jnp.arange(2 * REACH + 1, dtype=jnp.int32) - REACH)
    keep = (offsets[None, :] <= tap_windows[:, None]).astype(jnp.float32)
    return fringe_taps * keep[None, :, :]


def convolve(rows, slot_taps, length):
    real_part = jnp.zeros(rows.shape[1:2] + (length,) + rows.shape[3:], jnp.float32)
    imag_part = jnp.zeros_like(real_part)
    for offset in range(2 * REACH + 1):
        shifted = lax.slice_in_dim(rows, 2 * REACH - offset, 2 * REACH - offset + length, axis=2)
        tap_real = slot_taps[0, :, offset][:, None, None]
        tap_imag = slot_taps[1, :, offset][:, None, None]
        real_part = real_part + tap_real * shifted[0] - tap_imag * shifted[1]
        imag_part = imag_part + tap_real * shifted[1] + tap_imag * shifted[0]
    return jnp.stack([real_part, imag_part]).astype(jnp.bfloat16)


def convolve_class(rows, taps, count, length):
    live = (jnp.arange(rows.shape[1], dtype=jnp.int32) < count).astype(jnp.float32)
    return convolve(rows, taps[:, None, :] * live[None, :, None], length)


def to_slots(per_baseline, class_counts):
    class_starts = jnp.cumsum(class_counts) - class_counts
    slot_positions = jnp.arange(SLOTS, dtype=jnp.int32)
    input_visibility = jnp.clip(
        class_starts[:, None] + slot_positions[None, :], 0, per_baseline.shape[1] - 1
    )
    live_slot = slot_positions[None, :] < class_counts[:, None]
    gathered = jnp.take(per_baseline, input_visibility.reshape(-1), axis=1)
    gathered = gathered.reshape(per_baseline.shape[:1] + live_slot.shape + per_baseline.shape[2:])
    return jnp.where(live_slot[None, :, :, None, None], gathered, jnp.zeros((), per_baseline.dtype))


def two_stage(
    visibilities, class_ids, class_counts, tap_windows, fringe_taps, flag_mask, filter_panels
):
    taps_kept = masked_taps(fringe_taps, tap_windows)
    padded = extended(visibilities, (("tm", 2),), REACH)
    row_taps = taps_kept[:, class_ids, :]
    filtered = convolve(padded, row_taps, visibilities.shape[2])
    slotted = to_slots(filtered, class_counts)
    local_block = lax.all_to_all(
        lax.all_to_all(slotted, "tm", split_axis=1, concat_axis=3, tiled=True),
        "freq",
        split_axis=3,
        concat_axis=4,
        tiled=True,
    )
    weighted = local_block * flag_mask.astype(jnp.bfloat16)
    dayenu_fit = jnp.einsum(
        "rcstj,cij->rcsti",
        weighted,
        lax.all_gather(filter_panels, "freq", axis=1, tiled=True),
        preferred_element_type=jnp.float32,
    )
    return (local_block.astype(jnp.float32) - dayenu_fit).astype(jnp.bfloat16)


def shards(
    visibilities, class_ids, class_counts, tap_windows, fringe_taps, flag_mask, filter_panels
):
    nt = lax.axis_size("tm")
    nf = lax.axis_size("freq")
    if nt != nf:
        return two_stage(
            visibilities, class_ids, class_counts, tap_windows, fringe_taps, flag_mask,
            filter_panels,
        )
    q = nt // nf
    a = lax.axis_index("tm")
    b = lax.axis_index("freq")
    t_in = visibilities.shape[2]
    f_blk = visibilities.shape[3]
    t_out = flag_mask.shape[0]
    channels = flag_mask.shape[1]

    taps_kept = masked_taps(fringe_taps, tap_windows)
    class_starts = jnp.cumsum(class_counts) - class_counts

    padded = extended(visibilities, (("tm", 2),), REACH)
    padded = jnp.pad(padded, ((0, 0), (0, SLOTS), (0, 0), (0, 0)))

    if q == 1 and nf & (nf - 1) == 0:
        blocks = filter_panels[0][None]
        step = nf // 2
        while step >= 1:
            perm = [(f, f ^ step) for f in range(nf)]
            blocks = jnp.concatenate([blocks, lax.ppermute(blocks, "freq", perm)], axis=0)
            step //= 2
        codes = [0]
        step = nf // 2
        while step >= 1:
            codes = codes + [x ^ step for x in codes]
            step //= 2
        where = {code: m for m, code in enumerate(codes)}
        branches = [
            functools.partial(in_order, order=[where[k ^ own] for k in range(nf)])
            for own in range(nf)
        ]
        panel = lax.switch(b, branches, blocks)
    else:
        panel = lax.all_gather(filter_panels[0], "freq", axis=0, tiled=True)
    if q == 1:
        shift = ((a + 1) % nf) * f_blk
        panel = jnp.concatenate([panel, panel], axis=1)
        panel = lax.dynamic_slice_in_dim(panel, shift, channels, axis=1)

    c_own = a
    u_src = (a % q) * nf + b
    fit = None
    for r in list(range(1, nt)) + [0]:
        c_send = (u_src + r) % nt
        start = class_starts[c_send]
        rows = lax.dynamic_slice_in_dim(padded, start, SLOTS, axis=1)
        taps = lax.dynamic_index_in_dim(taps_kept, c_send, axis=1, keepdims=False)
        chunk = convolve_class(rows, taps, class_counts[c_send], t_in)
        perm = []
        for sa in range(nt):
            for sb in range(nf):
                u = (sa % q) * nf + sb
                dc = (u + r) % nt
                perm.append((sa * nf + sb, dc * nf + sa // q))
        got = lax.ppermute(chunk, ("tm", "freq"), perm)
        u_dst = (c_own - r) % nt
        t_sub = u_dst // nf
        b_src = u_dst % nf
        if q == 1:
            gate = lax.dynamic_slice_in_dim(flag_mask, b_src * f_blk, f_blk, axis=1)
            cols = lax.slice_in_dim(panel, (nf - 1 - r) * f_blk, (nf - r) * f_blk, axis=1)
        else:
            gate = lax.dynamic_slice(flag_mask, (t_sub * t_in, b_src * f_blk), (t_in, f_blk))
            cols = lax.dynamic_slice_in_dim(panel, b_src * f_blk, f_blk, axis=1)
        weighted = got * gate.astype(jnp.bfloat16)
        part = jnp.einsum("rstj,ij->rsti", weighted, cols, preferred_element_type=jnp.float32)
        if fit is None:
            slotted = jnp.zeros((2, SLOTS, t_out, channels), jnp.bfloat16)
        if q == 1:
            fit = part if fit is None else fit + part
            slotted = lax.dynamic_update_slice_in_dim(slotted, got, b_src * f_blk, axis=3)
        else:
            if fit is None:
                fit = jnp.zeros((2, SLOTS, t_out, channels), jnp.float32)
            prev = lax.dynamic_slice_in_dim(fit, t_sub * t_in, t_in, axis=2)
            fit = lax.dynamic_update_slice_in_dim(fit, prev + part, t_sub * t_in, axis=2)
            slotted = lax.dynamic_update_slice(slotted, got, (0, 0, t_sub * t_in, b_src * f_blk))
    cleaned = (slotted.astype(jnp.float32) - fit).astype(jnp.bfloat16)
    return cleaned[:, None]


def solution(mesh):
    return jax.shard_map(
        shards,
        mesh=mesh,
        in_specs=(
            P(None, "grp", "tm", "freq"),
            P("grp"),
            P("grp"),
            P("grp"),
            P(None, "grp", None),
            P("freq", None),
            P(("grp", "tm"), "freq", None),
        ),
        out_specs=P(None, ("grp", "tm"), None, "freq", None),
        check_vma=False,
    )
```
